512 devices in a mesh: ctx: 64 (over x, y, z_hi, core), head: 8 (over z_lo).
Axes of the slice: x: 4, y: 4, z: 16 (z_hi: 2, z_lo: 8; z = z_hi * 8 + z_lo), core: 2. Of those that a mesh axis runs over, the one named last changes fastest.
Arguments:
- query_head_rows: bfloat16 [16384, 4096], P('ctx', 'head'), may hold values from -4 to 4
- key_head_rows: bfloat16 [16384, 1024], P('ctx', 'head'), may hold values from -4 to 4
- value_head_rows: bfloat16 [16384, 1024], P('ctx', 'head'), may hold values from -4 to 4
- forward_output: bfloat16 [16384, 4096], P('ctx', 'head'), may hold values from -4 to 4, as said below
- cotangent: bfloat16 [16384, 4096], P('ctx', 'head'), may hold values from -6 to 6
- logsumexp: float32 [32, 16384], P('head', 'ctx'), as said below
- document_lengths: int32 [64], replicated, may hold values from 1 to 768, as said below
- linear_row_index: int32 [16384], replicated, may hold values from 0 to 16383, as said below
Outputs:
- query_gradient: bfloat16 [16384, 4096], P(('ctx', 'head'))
- linear_key_gradient: bfloat16 [16384, 1024], P(('ctx', 'head'))
- linear_value_gradient: bfloat16 [16384, 1024], P(('ctx', 'head'))
The draws below stay inside these ranges and needn't reach their ends.
Inputs may be any that keep to these rules, and one draw needn't show every extreme that they name: `logsumexp`: for each head and position, the log of the sum of exp(scores) over the keys that the position sees, from the forward pass on these query_head_rows and key_head_rows. `forward_output`: for each head, the forward pass's softmax weights times value_head_rows, rounded to bfloat16. `document_lengths`: the lengths sum to 16384; the longest document has exactly 768 tokens. `linear_row_index`: A permutation of the 16384 positions. Counting positions in blocks of 256, from one block of the packed sequence at most 8 rows go to one block of linear positions, some pair of blocks reaches 8, and every linear block receives 256 rows.
All inputs are finite; a program needn't handle non-finite values.
Results may differ from the reference program's by a relative error of at most 0.0049.
Values may be sent and summed in bfloat16 or wider, within the bound.
No kernel may reach another device: no remote copies, remote signals or barrier semaphores. Data moves between devices by JAX's collectives and lax.ppermute only.
A program may use at most 64 MiB of HBM per device.

```python
import jax
import jax.numpy as jnp
from jax import lax

QUERY_HEADS = 32
KEY_VALUE_HEADS = 8
HEAD_SIZE = 128
TOK_DEV = 256
DOC_BLOCKS = 3
PACKED_TOKENS = 16384
DOC = 768
NDOCS = 64
CAP = 8


def base_fields(key):
    field_keys = jax.random.split(jax.random.fold_in(key, 11), 4)
    document_spans = ((PACKED_TOKENS, QUERY_HEADS * HEAD_SIZE), (PACKED_TOKENS, KEY_VALUE_HEADS * HEAD_SIZE), (PACKED_TOKENS, KEY_VALUE_HEADS * HEAD_SIZE))
    fields = []
    for which in range(3):
        extent = document_spans[which]
        values = jnp.clip(jax.random.normal(field_keys[which], extent, jnp.float32), -4.0, 4.0)
        rounded = lax.optimization_barrier(values.astype(jnp.bfloat16)).astype(jnp.float32)
        fields.append(rounded)
    return fields


def length_draw(key):
    first_key, second_key = jax.random.split(key)
    spare = PACKED_TOKENS - DOC - (NDOCS - 1)
    weights = jax.random.randint(first_key, (NDOCS - 1,), 500, 1001).astype(jnp.int32)
    base = (1 + spare * weights // jnp.sum(weights)).astype(jnp.int32)
    short = PACKED_TOKENS - DOC - jnp.sum(base)
    base = base + (lax.iota(jnp.int32, NDOCS - 1) < short).astype(jnp.int32)
    chosen = jax.random.randint(second_key, (), 0, NDOCS)
    index = lax.iota(jnp.int32, NDOCS)
    source = jnp.clip(jnp.where(index < chosen, index, index - 1), 0, NDOCS - 2)
    return jnp.where(index == chosen, DOC, base[source]).astype(jnp.int32)


def attention_stats(key):
    query_full_rows, key_full_rows, value_full_rows = base_fields(key)
    lengths = length_draw(jax.random.fold_in(key, 5))
    query_groups = QUERY_HEADS // KEY_VALUE_HEADS
    scaling = HEAD_SIZE ** (-0.5)
    spare_border = DOC_BLOCKS * TOK_DEV
    window = spare_border + TOK_DEV
    finish = jnp.cumsum(lengths).astype(jnp.int32)
    firsts = finish - lengths
    positions = lax.iota(jnp.int32, PACKED_TOKENS)
    begins = jnp.max(jnp.where(firsts[None, :] <= positions[:, None], firsts[None, :], 0), axis=1)
    query_vectors = query_full_rows.reshape(PACKED_TOKENS, KEY_VALUE_HEADS, query_groups, HEAD_SIZE)
    padding_width = jnp.zeros((spare_border, KEY_VALUE_HEADS, HEAD_SIZE), jnp.float32)
    key_padded = jnp.concatenate([padding_width, key_full_rows.reshape(PACKED_TOKENS, KEY_VALUE_HEADS, HEAD_SIZE)], axis=0)
    value_padded = jnp.concatenate([padding_width, value_full_rows.reshape(PACKED_TOKENS, KEY_VALUE_HEADS, HEAD_SIZE)], axis=0)

    def one_block(block):
        first = (block * TOK_DEV).astype(jnp.int32)
        query_part = lax.dynamic_slice_in_dim(query_vectors, first, TOK_DEV)
        begin_part = lax.dynamic_slice_in_dim(begins, first, TOK_DEV)
        key_part = lax.dynamic_slice_in_dim(key_padded, first, window)
        value_part = lax.dynamic_slice_in_dim(value_padded, first, window)
        key_pos = first - spare_border + lax.iota(jnp.int32, window)
        query_pos = first + lax.iota(jnp.int32, TOK_DEV)
        visible = (key_pos[None, :] <= query_pos[:, None]) & (key_pos[None, :] >= begin_part[:, None])
        scores = jnp.einsum('qngd,knd->qngk', query_part, key_part) * scaling
        masked = jnp.where(visible[:, None, None, :], scores, -jnp.inf)
        top = jnp.max(masked, axis=3, keepdims=True)
        log_normalizer = top[..., 0] + jnp.log(jnp.sum(jnp.exp(masked - top), axis=3))
        weights = jnp.exp(masked - log_normalizer[..., None])
        outputs = jnp.einsum('qngk,knd->qngd', weights, value_part)
        return (log_normalizer, outputs)
    log_totals, outputs = lax.map(one_block, jnp.arange(PACKED_TOKENS // TOK_DEV, dtype=jnp.int32))
    return (log_totals.reshape(PACKED_TOKENS, QUERY_HEADS).T, outputs.reshape(PACKED_TOKENS, QUERY_HEADS * HEAD_SIZE))


def remap_draw(key):
    count = PACKED_TOKENS // TOK_DEV
    half = CAP // 2
    keys = jax.random.split(key, 5)
    shifts = jax.random.randint(keys[0], (count // 2,), -half, half + 1).astype(jnp.int32)
    shifts = shifts.at[0].set(half)
    loads = jnp.stack([half + shifts, half - shifts], axis=1).reshape(count)
    loads = loads[jax.random.permutation(keys[1], count)]
    labels = jax.random.permutation(keys[2], count).astype(jnp.int32)
    matrix = loads[(labels[None, :] - labels[:, None]) % count].astype(jnp.int32)
    inclusive = jnp.cumsum(matrix, axis=1).astype(jnp.int32)
    exclusive = inclusive - matrix
    places = lax.iota(jnp.int32, TOK_DEV)
    owner_of = jnp.sum((places[None, :, None] >= inclusive[:, None, :]).astype(jnp.int32), axis=2)
    ranks = places[None, :] - jnp.take_along_axis(exclusive, owner_of, axis=1)
    arrivals = (jnp.cumsum(matrix, axis=0) - matrix).astype(jnp.int32)
    slot_at = jnp.take_along_axis(arrivals, owner_of, axis=1) + ranks
    receive_order = jax.vmap(lambda sub: jax.random.permutation(sub, TOK_DEV))(jax.random.split(keys[3], count)).astype(jnp.int32)
    send_order = jax.vmap(lambda sub: jax.random.permutation(sub, TOK_DEV))(jax.random.split(keys[4], count)).astype(jnp.int32)
    position = receive_order[owner_of, slot_at]
    targets = owner_of * TOK_DEV + position
    sources = lax.iota(jnp.int32, count)[:, None] * TOK_DEV + send_order
    return jnp.zeros((PACKED_TOKENS,), jnp.int32).at[sources.reshape(-1)].set(targets.reshape(-1).astype(jnp.int32))


def draw_query_head_rows(key, part):
    return base_fields(key)[0].astype(jnp.bfloat16)


def draw_key_head_rows(key, part):
    return base_fields(key)[1].astype(jnp.bfloat16)


def draw_value_head_rows(key, part):
    return base_fields(key)[2].astype(jnp.bfloat16)


def draw_logsumexp(key, part):
    return attention_stats(key)[0].astype(jnp.float32)


def draw_forward_output(key, part):
    return attention_stats(key)[1].astype(jnp.bfloat16)


def draw_document_lengths(key, part):
    return length_draw(jax.random.fold_in(key, 5)).astype(jnp.int32)


def draw_linear_row_index(key, part):
    return remap_draw(jax.random.fold_in(key, 3)).astype(jnp.int32)


def levels(key, dims, pieces, least, high):
    def one(axis_at, parts):
        draws = jax.random.uniform(jax.random.fold_in(jax.random.fold_in(key, 6), axis_at), (parts,), jnp.float32, least / len(pieces), high / len(pieces))
        return jnp.repeat(jnp.exp(draws), dims[axis_at] // parts).reshape((-1,) + (1,) * (len(dims) - axis_at - 1))

    level = one(*pieces[0])
    for cut in pieces[1:]:
        level = level * one(*cut)
    return level


def normal_values(stream_key, shape, width, bound, cuts=(), kind=jnp.bfloat16):
    values = width * jax.random.normal(stream_key, shape, jnp.float32)
    if cuts:
        values = values * levels(stream_key, shape, cuts, -0.22, 0.18)
    return jnp.clip(values, -bound, bound).astype(kind)


def setup_inputs(seed: int = 0) -> dict:
    key_list = jax.random.split(jax.random.key(seed), 9)
    return {
        "query_head_rows": draw_query_head_rows(jax.random.fold_in(key_list[8], 71), 0),
        "key_head_rows": draw_key_head_rows(jax.random.fold_in(key_list[8], 71), 0),
        "value_head_rows": draw_value_head_rows(jax.random.fold_in(key_list[8], 71), 0),
        "forward_output": draw_forward_output(jax.random.fold_in(key_list[8], 71), 0),
        "cotangent": normal_values(key_list[4], (PACKED_TOKENS, QUERY_HEADS * HEAD_SIZE), 1.0, 6.0, ((0, 64), (1, 8))),
        "logsumexp": draw_logsumexp(jax.random.fold_in(key_list[8], 71), 0),
        "document_lengths": draw_document_lengths(jax.random.fold_in(key_list[8], 71), 0),
        "linear_row_index": draw_linear_row_index(jax.random.fold_in(key_list[8], 71), 0),
    }


def document_begins(document_lengths, positions):
    finish = jnp.cumsum(document_lengths).astype(jnp.int32)
    firsts = (finish - document_lengths).astype(jnp.int32)
    chosen = jnp.where(firsts[None, :] <= positions[:, None], firsts[None, :], 0)
    return jnp.max(chosen, axis=1).astype(jnp.int32)


def reference(query_head_rows, key_head_rows, value_head_rows, forward_output, cotangent, logsumexp, document_lengths, linear_row_index):
    query_groups = QUERY_HEADS // KEY_VALUE_HEADS
    scaling = HEAD_SIZE ** -0.5
    spare_border = DOC_BLOCKS * TOK_DEV
    window = spare_border + TOK_DEV
    positions = lax.iota(jnp.int32, PACKED_TOKENS)
    begins = document_begins(document_lengths, positions)
    query_vectors = query_head_rows.astype(jnp.float32).reshape(PACKED_TOKENS, KEY_VALUE_HEADS, query_groups, HEAD_SIZE)
    output_gradient = cotangent.astype(jnp.float32).reshape(PACKED_TOKENS, KEY_VALUE_HEADS, query_groups, HEAD_SIZE)
    log_normalizer = logsumexp.T.reshape(PACKED_TOKENS, KEY_VALUE_HEADS, query_groups)
    row_correction = jnp.sum(output_gradient * forward_output.astype(jnp.float32).reshape(PACKED_TOKENS, KEY_VALUE_HEADS, query_groups, HEAD_SIZE), axis=3)
    padding_width = jnp.zeros((spare_border, KEY_VALUE_HEADS, HEAD_SIZE), jnp.float32)
    key_padded = jnp.concatenate([padding_width, key_head_rows.astype(jnp.float32).reshape(PACKED_TOKENS, KEY_VALUE_HEADS, HEAD_SIZE)], axis=0)
    value_padded = jnp.concatenate([padding_width, value_head_rows.astype(jnp.float32).reshape(PACKED_TOKENS, KEY_VALUE_HEADS, HEAD_SIZE)], axis=0)

    def one_block(carry, block):
        key_running_sum, value_running_sum = carry
        first = (block * TOK_DEV).astype(jnp.int32)
        query_part = lax.dynamic_slice_in_dim(query_vectors, first, TOK_DEV)
        grad_part = lax.dynamic_slice_in_dim(output_gradient, first, TOK_DEV)
        total_part = lax.dynamic_slice_in_dim(log_normalizer, first, TOK_DEV)
        delta_part = lax.dynamic_slice_in_dim(row_correction, first, TOK_DEV)
        begin_part = lax.dynamic_slice_in_dim(begins, first, TOK_DEV)
        key_part = lax.dynamic_slice_in_dim(key_padded, first, window)
        value_part = lax.dynamic_slice_in_dim(value_padded, first, window)
        key_pos = first - spare_border + lax.iota(jnp.int32, window)
        query_pos = first + lax.iota(jnp.int32, TOK_DEV)
        visible = (key_pos[None, :] <= query_pos[:, None]) & (key_pos[None, :] >= begin_part[:, None])
        scores = jnp.einsum("qngd,knd->qngk", query_part, key_part) * scaling
        weights = jnp.exp(jnp.where(visible[:, None, None, :], scores - total_part[..., None], -jnp.inf))
        weights_low = lax.optimization_barrier(weights.astype(jnp.bfloat16)).astype(jnp.float32)
        grad_weights = jnp.einsum("qngd,knd->qngk", grad_part, value_part)
        grad_scores = (weights * (grad_weights - delta_part[..., None]) * scaling).astype(jnp.bfloat16)
        grad_scores = lax.optimization_barrier(grad_scores).astype(jnp.float32)
        query_term = jnp.einsum("qngk,knd->qngd", grad_scores, key_part)
        key_term = jnp.einsum("qngk,qngd->knd", grad_scores, query_part)
        value_term = jnp.einsum("qngk,qngd->knd", weights_low, grad_part)
        key_running_sum = lax.dynamic_update_slice_in_dim(key_running_sum, lax.dynamic_slice_in_dim(key_running_sum, first, window) + key_term, first, 0)
        value_running_sum = lax.dynamic_update_slice_in_dim(value_running_sum, lax.dynamic_slice_in_dim(value_running_sum, first, window) + value_term, first, 0)
        return (key_running_sum, value_running_sum), query_term.astype(jnp.bfloat16)

    start_running_sum = jnp.zeros((PACKED_TOKENS + spare_border, KEY_VALUE_HEADS, HEAD_SIZE), jnp.float32)
    block_ids = jnp.arange(PACKED_TOKENS // TOK_DEV, dtype=jnp.int32)
    (key_running_sum, value_running_sum), query_blocks = lax.scan(one_block, (start_running_sum, start_running_sum), block_ids)
    query_grad = query_blocks.reshape(PACKED_TOKENS, QUERY_HEADS * HEAD_SIZE)
    key_row_gradient = key_running_sum[spare_border:].reshape(PACKED_TOKENS, KEY_VALUE_HEADS * HEAD_SIZE).astype(jnp.bfloat16)
    value_row_gradient = value_running_sum[spare_border:].reshape(PACKED_TOKENS, KEY_VALUE_HEADS * HEAD_SIZE).astype(jnp.bfloat16)
    query_gradient = jnp.zeros((PACKED_TOKENS, QUERY_HEADS * HEAD_SIZE), jnp.bfloat16).at[linear_row_index].set(query_grad)
    linear_key_gradient = jnp.zeros((PACKED_TOKENS, KEY_VALUE_HEADS * HEAD_SIZE), jnp.bfloat16).at[linear_row_index].set(key_row_gradient)
    linear_value_gradient = jnp.zeros((PACKED_TOKENS, KEY_VALUE_HEADS * HEAD_SIZE), jnp.bfloat16).at[linear_row_index].set(value_row_gradient)
    return (query_gradient, linear_key_gradient, linear_value_gradient)
```

```python
import jax
import jax.numpy as jnp
from jax import lax
from jax.sharding import PartitionSpec as P

HEAD_SIZE = 128
DOC_BLOCKS = 3


def from_behind(shard, axis, by):
    count = lax.axis_size(axis)
    pairs = [(i, i + by) for i in range(count) if 0 <= i + by < count]
    return lax.ppermute(shard, axis, pairs)


def block_grads(
    query_vectors,
    output_gradient,
    log_normalizer,
    row_correction,
    begins,
    query_pos,
    key_heads,
    value_heads,
    key_start,
):
    length = query_vectors.shape[0]
    scaling = HEAD_SIZE ** (-0.5)
    scores = (
        jnp.einsum("qngd,knd->qngk", query_vectors, key_heads, preferred_element_type=jnp.float32)
        * scaling
    )
    key_pos = key_start + lax.iota(jnp.int32, length)
    visible = (key_pos[None, :] <= query_pos[:, None]) & (key_pos[None, :] >= begins[:, None])
    weights = jnp.exp(
        jnp.where(visible[:, None, None, :], scores - log_normalizer[..., None], -jnp.inf)
    )
    weights_low = weights.astype(jnp.bfloat16)
    grad_weights = jnp.einsum(
        "qngd,knd->qngk", output_gradient, value_heads, preferred_element_type=jnp.float32
    )
    grad_scores = (weights * (grad_weights - row_correction[..., None]) * scaling).astype(
        jnp.bfloat16
    )
    query_term = jnp.einsum(
        "qngk,knd->qngd", grad_scores, key_heads, preferred_element_type=jnp.float32
    )
    key_term = jnp.einsum(
        "qngk,qngd->knd", grad_scores, query_vectors, preferred_element_type=jnp.float32
    )
    value_term = jnp.einsum(
        "qngk,qngd->knd", weights_low, output_gradient, preferred_element_type=jnp.float32
    )
    return query_term, key_term.reshape(length, -1), value_term.reshape(length, -1)


def per_device(
    query_head_rows,
    key_head_rows,
    value_head_rows,
    forward_output,
    cotangent,
    logsumexp,
    document_lengths,
    linear_row_index,
):
    length = query_head_rows.shape[0]
    kv_heads = key_head_rows.shape[1] // HEAD_SIZE
    kv_width = key_head_rows.shape[1]
    q_width = query_head_rows.shape[1]
    query_groups = logsumexp.shape[0] // kv_heads
    block_index = lax.axis_index("ctx")
    blocks = lax.axis_size("ctx")
    heads_axis = lax.axis_size("head")

    kv_own = jnp.concatenate([key_head_rows, value_head_rows], axis=1)
    kv_behind = [from_behind(kv_own, "ctx", d) for d in range(1, DOC_BLOCKS + 1)]

    query_pos = block_index * length + lax.iota(jnp.int32, length)
    finish = jnp.cumsum(document_lengths)
    firsts = finish - document_lengths
    begins = jnp.max(jnp.where(firsts[None, :] <= query_pos[:, None], firsts[None, :], 0), axis=1)
    query_vectors = query_head_rows.reshape(length, kv_heads, query_groups, HEAD_SIZE)
    output_gradient = cotangent.reshape(length, kv_heads, query_groups, HEAD_SIZE)
    log_normalizer = logsumexp.T.reshape(length, kv_heads, query_groups)
    row_correction = jnp.sum(
        output_gradient.astype(jnp.float32)
        * forward_output.reshape(length, kv_heads, query_groups, HEAD_SIZE).astype(jnp.float32),
        axis=3,
    )

    def block_terms(kv_part, distance):
        key_start = (block_index - distance) * length
        key_heads = kv_part[:, :kv_width].reshape(length, kv_heads, HEAD_SIZE)
        value_heads = kv_part[:, kv_width:].reshape(length, kv_heads, HEAD_SIZE)
        return block_grads(
            query_vectors,
            output_gradient,
            log_normalizer,
            row_correction,
            begins,
            query_pos,
            key_heads,
            value_heads,
            key_start,
        )

    query_acc, key_sum, value_sum = block_terms(kv_own, 0)
    returned = []
    for distance in range(1, DOC_BLOCKS + 1):
        query_term, key_term, value_term = block_terms(kv_behind[distance - 1], distance)
        query_acc = query_acc + query_term
        partial = jnp.concatenate([key_term, value_term], axis=1)
        returned.append(from_behind(partial, "ctx", -distance))
    for part in returned:
        key_sum = key_sum + part[:, :kv_width]
        value_sum = value_sum + part[:, kv_width:]

    rows = jnp.concatenate(
        [
            query_acc.reshape(length, -1).astype(jnp.bfloat16),
            key_sum.astype(jnp.bfloat16),
            value_sum.astype(jnp.bfloat16),
        ],
        axis=1,
    )
    width = rows.shape[1]

    capacity = 2 * length // blocks
    own_targets = lax.dynamic_slice_in_dim(linear_row_index, block_index * length, length)
    target = own_targets // length
    owner_marks = (target[:, None] == lax.iota(jnp.int32, blocks)[None, :]).astype(jnp.int32)
    slot_rank = jnp.sum(owner_marks * (jnp.cumsum(owner_marks, axis=0) - 1), axis=1)
    send_slots = target * capacity + slot_rank
    pack = (
        lax.iota(jnp.int32, blocks * capacity)[:, None] == send_slots[None, :]
    ).astype(jnp.bfloat16)
    packed = jnp.dot(pack, rows, preferred_element_type=jnp.float32).astype(jnp.bfloat16)

    arrived = lax.all_to_all(packed, "ctx", split_axis=0, concat_axis=0, tiled=True)

    all_owners = linear_row_index.reshape(blocks, length)
    landing = all_owners // length == block_index
    landed_rank = jnp.cumsum(landing.astype(jnp.int32), axis=1) - 1
    where_to = all_owners % length
    chosen = landing[:, :, None] & (
        landed_rank[:, :, None] == lax.iota(jnp.int32, capacity)[None, None, :]
    )
    slot_pos = jnp.sum(jnp.where(chosen, where_to[:, :, None], 0), axis=1).reshape(-1)
    slot_valid = jnp.any(chosen, axis=1).reshape(-1)
    unpack = (
        (lax.iota(jnp.int32, length)[:, None] == slot_pos[None, :]) & slot_valid[None, :]
    ).astype(jnp.bfloat16)
    linear_rows = jnp.dot(unpack, arrived, preferred_element_type=jnp.float32).astype(
        jnp.bfloat16
    )

    gathered = lax.all_to_all(linear_rows, "head", split_axis=0, concat_axis=1, tiled=True)
    sub = length // heads_axis
    gathered = gathered.reshape(sub, heads_axis, width)
    query_out = gathered[:, :, :q_width].reshape(sub, heads_axis * q_width)
    key_out = gathered[:, :, q_width : q_width + kv_width].reshape(sub, heads_axis * kv_width)
    value_out = gathered[:, :, q_width + kv_width :].reshape(sub, heads_axis * kv_width)
    return query_out, key_out, value_out


def solution(mesh):
    placed = (
        P("ctx", "head"),
        P("ctx", "head"),
        P("ctx", "head"),
        P("ctx", "head"),
        P("ctx", "head"),
        P("head", "ctx"),
        P(),
        P(),
    )
    return jax.shard_map(
        per_device,
        mesh=mesh,
        in_specs=placed,
        out_specs=(P(("ctx", "head"), None), P(("ctx", "head"), None), P(("ctx", "head"), None)),
        check_vma=False,
    )
```

```python
import jax
import jax.numpy as jnp
from jax import lax
from jax.sharding import PartitionSpec as P

HEAD_SIZE = 128
DOC_BLOCKS = 3


def from_behind(shard, axis, by):
    count = lax.axis_size(axis)
    pairs = [(i, i + by) for i in range(count) if 0 <= i + by < count]
    return lax.ppermute(shard, axis, pairs)


def block_grads(
    query_vectors,
    output_gradient,
    log_normalizer,
    row_correction,
    begins,
    query_pos,
    key_heads,
    value_heads,
    key_start,
):
    length = query_vectors.shape[0]
    scaling = HEAD_SIZE ** (-0.5)
    scores = (
        jnp.einsum("qngd,knd->qngk", query_vectors, key_heads, preferred_element_type=jnp.float32)
        * scaling
    )
    key_pos = key_start + lax.iota(jnp.int32, length)
    visible = (key_pos[None, :] <= query_pos[:, None]) & (key_pos[None, :] >= begins[:, None])
    weights = jnp.exp(
        jnp.where(visible[:, None, None, :], scores - log_normalizer[..., None], -jnp.inf)
    )
    weights_low = weights.astype(jnp.bfloat16)
    grad_weights = jnp.einsum(
        "qngd,knd->qngk", output_gradient, value_heads, preferred_element_type=jnp.float32
    )
    grad_scores = (weights * (grad_weights - row_correction[..., None]) * scaling).astype(
        jnp.bfloat16
    )
    query_term = jnp.einsum(
        "qngk,knd->qngd", grad_scores, key_heads, preferred_element_type=jnp.float32
    )
    key_term = jnp.einsum(
        "qngk,qngd->knd", grad_scores, query_vectors, preferred_element_type=jnp.float32
    )
    value_term = jnp.einsum(
        "qngk,qngd->knd", weights_low, output_gradient, preferred_element_type=jnp.float32
    )
    return query_term, key_term.reshape(length, -1), value_term.reshape(length, -1)


def per_device(
    query_head_rows,
    key_head_rows,
    value_head_rows,
    forward_output,
    cotangent,
    logsumexp,
    document_lengths,
    linear_row_index,
):
    length = query_head_rows.shape[0]
    kv_heads = key_head_rows.shape[1] // HEAD_SIZE
    kv_width = key_head_rows.shape[1]
    q_width = query_head_rows.shape[1]
    query_groups = logsumexp.shape[0] // kv_heads
    block_index = lax.axis_index("ctx")
    blocks = lax.axis_size("ctx")
    heads_axis = lax.axis_size("head")

    kv_own = jnp.concatenate([key_head_rows, value_head_rows], axis=1)
    kv_behind = [from_behind(kv_own, "ctx", d) for d in range(1, DOC_BLOCKS + 1)]

    query_pos = block_index * length + lax.iota(jnp.int32, length)
    finish = jnp.cumsum(document_lengths)
    firsts = finish - document_lengths
    begins = jnp.max(jnp.where(firsts[None, :] <= query_pos[:, None], firsts[None, :], 0), axis=1)
    query_vectors = query_head_rows.reshape(length, kv_heads, query_groups, HEAD_SIZE)
    output_gradient = cotangent.reshape(length, kv_heads, query_groups, HEAD_SIZE)
    log_normalizer = logsumexp.T.reshape(length, kv_heads, query_groups)
    row_correction = jnp.sum(
        output_gradient.astype(jnp.float32)
        * forward_output.reshape(length, kv_heads, query_groups, HEAD_SIZE).astype(jnp.float32),
        axis=3,
    )

    def block_terms(kv_part, distance):
        key_start = (block_index - distance) * length
        key_heads = kv_part[:, :kv_width].reshape(length, kv_heads, HEAD_SIZE)
        value_heads = kv_part[:, kv_width:].reshape(length, kv_heads, HEAD_SIZE)
        return block_grads(
            query_vectors,
            output_gradient,
            log_normalizer,
            row_correction,
            begins,
            query_pos,
            key_heads,
            value_heads,
            key_start,
        )

    query_acc, key_sum, value_sum = block_terms(kv_own, 0)
    returned = []
    for distance in range(1, DOC_BLOCKS + 1):
        query_term, key_term, value_term = block_terms(kv_behind[distance - 1], distance)
        query_acc = query_acc + query_term
        partial = jnp.concatenate([key_term, value_term], axis=1).astype(jnp.bfloat16)
        returned.append(from_behind(partial, "ctx", -distance))
    for part in returned:
        key_sum = key_sum + part[:, :kv_width].astype(jnp.float32)
        value_sum = value_sum + part[:, kv_width:].astype(jnp.float32)

    rows = jnp.concatenate(
        [
            query_acc.reshape(length, -1).astype(jnp.bfloat16),
            key_sum.astype(jnp.bfloat16),
            value_sum.astype(jnp.bfloat16),
        ],
        axis=1,
    )
    width = rows.shape[1]

    capacity = 2 * length // blocks
    own_targets = lax.dynamic_slice_in_dim(linear_row_index, block_index * length, length)
    target = own_targets // length
    owner_marks = (target[:, None] == lax.iota(jnp.int32, blocks)[None, :]).astype(jnp.int32)
    slot_rank = jnp.sum(owner_marks * (jnp.cumsum(owner_marks, axis=0) - 1), axis=1)
    send_slots = target * capacity + slot_rank
    pack = (
        lax.iota(jnp.int32, blocks * capacity)[:, None] == send_slots[None, :]
    ).astype(jnp.bfloat16)
    packed = jnp.dot(pack, rows, preferred_element_type=jnp.float32).astype(jnp.bfloat16)

    arrived = lax.all_to_all(packed, "ctx", split_axis=0, concat_axis=0, tiled=True)

    all_owners = linear_row_index.reshape(blocks, length)
    landing = all_owners // length == block_index
    landed_rank = jnp.cumsum(landing.astype(jnp.int32), axis=1) - 1
    where_to = all_owners % length
    chosen = landing[:, :, None] & (
        landed_rank[:, :, None] == lax.iota(jnp.int32, capacity)[None, None, :]
    )
    slot_pos = jnp.sum(jnp.where(chosen, where_to[:, :, None], 0), axis=1).reshape(-1)
    slot_valid = jnp.any(chosen, axis=1).reshape(-1)
    unpack = (
        (lax.iota(jnp.int32, length)[:, None] == slot_pos[None, :]) & slot_valid[None, :]
    ).astype(jnp.bfloat16)
    linear_rows = jnp.dot(unpack, arrived, preferred_element_type=jnp.float32).astype(
        jnp.bfloat16
    )

    gathered = lax.all_to_all(linear_rows, "head", split_axis=0, concat_axis=1, tiled=True)
    sub = length // heads_axis
    gathered = gathered.reshape(sub, heads_axis, width)
    query_out = gathered[:, :, :q_width].reshape(sub, heads_axis * q_width)
    key_out = gathered[:, :, q_width : q_width + kv_width].reshape(sub, heads_axis * kv_width)
    value_out = gathered[:, :, q_width + kv_width :].reshape(sub, heads_axis * kv_width)
    return query_out, key_out, value_out


def solution(mesh):
    placed = (
        P("ctx", "head"),
        P("ctx", "head"),
        P("ctx", "head"),
        P("ctx", "head"),
        P("ctx", "head"),
        P("head", "ctx"),
        P(),
        P(),
    )
    return jax.shard_map(
        per_device,
        mesh=mesh,
        in_specs=placed,
        out_specs=(P(("ctx", "head"), None), P(("ctx", "head"), None), P(("ctx", "head"), None)),
        check_vma=False,
    )
```

```python
import jax
import jax.numpy as jnp
from jax import lax
from jax.sharding import PartitionSpec as P

HEAD_SIZE = 128
DOC_BLOCKS = 3


def from_behind(shard, axis, by):
    count = lax.axis_size(axis)
    pairs = [(i, i + by) for i in range(count) if 0 <= i + by < count]
    return lax.ppermute(shard, axis, pairs)


def block_grads(
    query_vectors,
    output_gradient,
    log_normalizer,
    row_correction,
    begins,
    query_pos,
    key_heads,
    value_heads,
    key_start,
):
    length = query_vectors.shape[0]
    scaling = HEAD_SIZE ** (-0.5)
    scores = (
        jnp.einsum("qngd,knd->qngk", query_vectors, key_heads, preferred_element_type=jnp.float32)
        * scaling
    )
    key_pos = key_start + lax.iota(jnp.int32, length)
    visible = (key_pos[None, :] <= query_pos[:, None]) & (key_pos[None, :] >= begins[:, None])
    weights = jnp.exp(
        jnp.where(visible[:, None, None, :], scores - log_normalizer[..., None], -jnp.inf)
    )
    weights_low = weights.astype(jnp.bfloat16)
    grad_weights = jnp.einsum(
        "qngd,knd->qngk", output_gradient, value_heads, preferred_element_type=jnp.float32
    )
    grad_scores = (weights * (grad_weights - row_correction[..., None]) * scaling).astype(
        jnp.bfloat16
    )
    query_term = jnp.einsum(
        "qngk,knd->qngd", grad_scores, key_heads, preferred_element_type=jnp.float32
    )
    key_term = jnp.einsum(
        "qngk,qngd->knd", grad_scores, query_vectors, preferred_element_type=jnp.float32
    )
    value_term = jnp.einsum(
        "qngk,qngd->knd", weights_low, output_gradient, preferred_element_type=jnp.float32
    )
    return query_term, key_term.reshape(length, -1), value_term.reshape(length, -1)


def per_device(
    query_head_rows,
    key_head_rows,
    value_head_rows,
    forward_output,
    cotangent,
    logsumexp,
    document_lengths,
    linear_row_index,
):
    length = query_head_rows.shape[0]
    kv_heads = key_head_rows.shape[1] // HEAD_SIZE
    kv_width = key_head_rows.shape[1]
    q_width = query_head_rows.shape[1]
    query_groups = logsumexp.shape[0] // kv_heads
    block_index = lax.axis_index("ctx")
    blocks = lax.axis_size("ctx")
    heads_axis = lax.axis_size("head")

    kv_own = jnp.concatenate([key_head_rows, value_head_rows], axis=1)
    even = block_index % 2 == 0
    partner = [(i, i ^ 1) for i in range(blocks)]
    kv_two = from_behind(kv_own, "ctx", 2)
    kv_partner_own = lax.ppermute(kv_own, "ctx", [(i, i + 1) for i in range(0, blocks, 2)])
    kv_partner_two = lax.ppermute(kv_two, "ctx", partner)
    kv_three = lax.ppermute(
        kv_own, "ctx", [(i, i + 3) for i in range(1, blocks, 2) if i + 3 < blocks]
    )
    kv_behind = [
        jnp.where(even, kv_partner_two, kv_partner_own),
        kv_two,
        jnp.where(even, kv_three, kv_partner_two),
    ]

    query_pos = block_index * length + lax.iota(jnp.int32, length)
    finish = jnp.cumsum(document_lengths)
    firsts = finish - document_lengths
    begins = jnp.max(jnp.where(firsts[None, :] <= query_pos[:, None], firsts[None, :], 0), axis=1)
    query_vectors = query_head_rows.reshape(length, kv_heads, query_groups, HEAD_SIZE)
    output_gradient = cotangent.reshape(length, kv_heads, query_groups, HEAD_SIZE)
    log_normalizer = logsumexp.T.reshape(length, kv_heads, query_groups)
    row_correction = jnp.sum(
        output_gradient.astype(jnp.float32)
        * forward_output.reshape(length, kv_heads, query_groups, HEAD_SIZE).astype(jnp.float32),
        axis=3,
    )

    def block_terms(kv_part, distance):
        key_start = (block_index - distance) * length
        key_heads = kv_part[:, :kv_width].reshape(length, kv_heads, HEAD_SIZE)
        value_heads = kv_part[:, kv_width:].reshape(length, kv_heads, HEAD_SIZE)
        return block_grads(
            query_vectors,
            output_gradient,
            log_normalizer,
            row_correction,
            begins,
            query_pos,
            key_heads,
            value_heads,
            key_start,
        )

    query_acc, key_sum, value_sum = block_terms(kv_own, 0)
    partials = []
    for distance in range(1, DOC_BLOCKS + 1):
        query_term, key_term, value_term = block_terms(kv_behind[distance - 1], distance)
        query_acc = query_acc + query_term
        partials.append(jnp.concatenate([key_term, value_term], axis=1))
    swapped = lax.ppermute(jnp.where(even, partials[0], partials[2]), "ctx", partner)
    to_partner = lax.ppermute(partials[0], "ctx", [(i, i - 1) for i in range(1, blocks, 2)])
    crossed = from_behind((partials[1] + swapped).astype(jnp.bfloat16), "ctx", -2)
    from_three = lax.ppermute(
        partials[2].astype(jnp.bfloat16), "ctx", [(i, i - 3) for i in range(0, blocks, 2) if i >= 3]
    )
    own_sum = jnp.concatenate([key_sum, value_sum], axis=1) + crossed.astype(jnp.float32)
    own_sum = own_sum + jnp.where(even, to_partner, from_three.astype(jnp.float32))
    key_sum = own_sum[:, :kv_width]
    value_sum = own_sum[:, kv_width:]

    rows = jnp.concatenate(
        [
            query_acc.reshape(length, -1).astype(jnp.bfloat16),
            key_sum.astype(jnp.bfloat16),
            value_sum.astype(jnp.bfloat16),
        ],
        axis=1,
    )
    width = rows.shape[1]

    capacity = 2 * length // blocks
    own_targets = lax.dynamic_slice_in_dim(linear_row_index, block_index * length, length)
    target = own_targets // length
    owner_marks = (target[:, None] == lax.iota(jnp.int32, blocks)[None, :]).astype(jnp.int32)
    slot_rank = jnp.sum(owner_marks * (jnp.cumsum(owner_marks, axis=0) - 1), axis=1)
    send_slots = target * capacity + slot_rank
    pack = (
        lax.iota(jnp.int32, blocks * capacity)[:, None] == send_slots[None, :]
    ).astype(jnp.bfloat16)
    packed = jnp.dot(pack, rows, preferred_element_type=jnp.float32).astype(jnp.bfloat16)

    arrived = lax.all_to_all(packed, "ctx", split_axis=0, concat_axis=0, tiled=True)

    all_owners = linear_row_index.reshape(blocks, length)
    landing = all_owners // length == block_index
    landed_rank = jnp.cumsum(landing.astype(jnp.int32), axis=1) - 1
    where_to = all_owners % length
    chosen = landing[:, :, None] & (
        landed_rank[:, :, None] == lax.iota(jnp.int32, capacity)[None, None, :]
    )
    slot_pos = jnp.sum(jnp.where(chosen, where_to[:, :, None], 0), axis=1).reshape(-1)
    slot_valid = jnp.any(chosen, axis=1).reshape(-1)
    unpack = (
        (lax.iota(jnp.int32, length)[:, None] == slot_pos[None, :]) & slot_valid[None, :]
    ).astype(jnp.bfloat16)
    linear_rows = jnp.dot(unpack, arrived, preferred_element_type=jnp.float32).astype(
        jnp.bfloat16
    )

    gathered = lax.all_to_all(linear_rows, "head", split_axis=0, concat_axis=1, tiled=True)
    sub = length // heads_axis
    gathered = gathered.reshape(sub, heads_axis, width)
    query_out = gathered[:, :, :q_width].reshape(sub, heads_axis * q_width)
    key_out = gathered[:, :, q_width : q_width + kv_width].reshape(sub, heads_axis * kv_width)
    value_out = gathered[:, :, q_width + kv_width :].reshape(sub, heads_axis * kv_width)
    return query_out, key_out, value_out


def solution(mesh):
    placed = (
        P("ctx", "head"),
        P("ctx", "head"),
        P("ctx", "head"),
        P("ctx", "head"),
        P("ctx", "head"),
        P("head", "ctx"),
        P(),
        P(),
    )
    return jax.shard_map(
        per_device,
        mesh=mesh,
        in_specs=placed,
        out_specs=(P(("ctx", "head"), None), P(("ctx", "head"), None), P(("ctx", "head"), None)),
        check_vma=False,
    )
```

```python
import jax
import jax.numpy as jnp
from jax import lax
from jax.sharding import PartitionSpec as P

HEAD_SIZE = 128
DOC_BLOCKS = 3


def from_behind(shard, axis, by):
    count = lax.axis_size(axis)
    pairs = [(i, i + by) for i in range(count) if 0 <= i + by < count]
    return lax.ppermute(shard, axis, pairs)


def block_grads(
    query_vectors,
    output_gradient,
    log_normalizer,
    row_correction,
    begins,
    query_pos,
    key_heads,
    value_heads,
    key_start,
):
    length = query_vectors.shape[0]
    scaling = HEAD_SIZE ** (-0.5)
    scores = (
        jnp.einsum("qngd,knd->qngk", query_vectors, key_heads, preferred_element_type=jnp.float32)
        * scaling
    )
    key_pos = key_start + lax.iota(jnp.int32, length)
    visible = (key_pos[None, :] <= query_pos[:, None]) & (key_pos[None, :] >= begins[:, None])
    weights = jnp.exp(
        jnp.where(visible[:, None, None, :], scores - log_normalizer[..., None], -jnp.inf)
    )
    weights_low = weights.astype(jnp.bfloat16)
    grad_weights = jnp.einsum(
        "qngd,knd->qngk", output_gradient, value_heads, preferred_element_type=jnp.float32
    )
    grad_scores = (weights * (grad_weights - row_correction[..., None]) * scaling).astype(
        jnp.bfloat16
    )
    query_term = jnp.einsum(
        "qngk,knd->qngd", grad_scores, key_heads, preferred_element_type=jnp.float32
    )
    key_term = jnp.einsum(
        "qngk,qngd->knd", grad_scores, query_vectors, preferred_element_type=jnp.float32
    )
    value_term = jnp.einsum(
        "qngk,qngd->knd", weights_low, output_gradient, preferred_element_type=jnp.float32
    )
    return query_term, key_term.reshape(length, -1), value_term.reshape(length, -1)


def per_device(
    query_head_rows,
    key_head_rows,
    value_head_rows,
    forward_output,
    cotangent,
    logsumexp,
    document_lengths,
    linear_row_index,
):
    length = query_head_rows.shape[0]
    kv_heads = key_head_rows.shape[1] // HEAD_SIZE
    kv_width = key_head_rows.shape[1]
    q_width = query_head_rows.shape[1]
    query_groups = logsumexp.shape[0] // kv_heads
    block_index = lax.axis_index("ctx")
    blocks = lax.axis_size("ctx")
    heads_axis = lax.axis_size("head")

    kv_own = jnp.concatenate([key_head_rows, value_head_rows], axis=1)
    even = block_index % 2 == 0
    partner = [(i, i ^ 1) for i in range(blocks)]
    kv_two = from_behind(kv_own, "ctx", 2)
    kv_three = lax.ppermute(
        kv_own, "ctx", [(i, i + 3) for i in range(1, blocks, 2) if i + 3 < blocks]
    )

    def query_side(index, rows_q, rows_do, lse, correction):
        positions = index * length + lax.iota(jnp.int32, length)
        finish = jnp.cumsum(document_lengths)
        firsts = finish - document_lengths
        starts = jnp.max(
            jnp.where(firsts[None, :] <= positions[:, None], firsts[None, :], 0), axis=1
        )
        return (
            rows_q.reshape(length, kv_heads, query_groups, HEAD_SIZE),
            rows_do.reshape(length, kv_heads, query_groups, HEAD_SIZE),
            lse.T.reshape(length, kv_heads, query_groups),
            correction,
            starts,
            positions,
        )

    row_correction = jnp.sum(
        cotangent.reshape(length, kv_heads, query_groups, HEAD_SIZE).astype(jnp.float32)
        * forward_output.reshape(length, kv_heads, query_groups, HEAD_SIZE).astype(jnp.float32),
        axis=3,
    )
    mine = query_side(block_index, query_head_rows, cotangent, logsumexp, row_correction)
    theirs_rows = lax.ppermute(
        (query_head_rows, cotangent, logsumexp, row_correction), "ctx", partner
    )
    theirs = query_side(block_index ^ 1, *theirs_rows)

    def block_terms(side, kv_part, key_block):
        key_heads = kv_part[:, :kv_width].reshape(length, kv_heads, HEAD_SIZE)
        value_heads = kv_part[:, kv_width:].reshape(length, kv_heads, HEAD_SIZE)
        query_term, key_term, value_term = block_grads(
            *side, key_heads, value_heads, key_block * length
        )
        return query_term, jnp.concatenate([key_term, value_term], axis=1)

    q_own, kv_grad_own = block_terms(mine, kv_own, block_index)
    q_two, kv_grad_two = block_terms(mine, kv_two, block_index - 2)
    q_cross, kv_grad_cross = block_terms(theirs, kv_two, block_index - 2)
    q_three, kv_grad_three = block_terms(mine, kv_three, block_index - 3)
    q_next, kv_grad_next = block_terms(theirs, kv_own, block_index)

    zero_q = jnp.zeros_like(q_own)
    zero_kv = jnp.zeros_like(kv_grad_own)
    sent_q = q_cross + jnp.where(even, q_next, zero_q)
    back_q = lax.ppermute(sent_q, "ctx", partner)
    query_acc = q_own + q_two + jnp.where(even, q_three, zero_q) + back_q

    crossed = from_behind((kv_grad_two + kv_grad_cross).astype(jnp.bfloat16), "ctx", -2)
    from_three = lax.ppermute(
        kv_grad_three.astype(jnp.bfloat16),
        "ctx",
        [(i, i - 3) for i in range(0, blocks, 2) if i >= 3],
    )
    own_sum = kv_grad_own + crossed.astype(jnp.float32)
    own_sum = own_sum + jnp.where(even, kv_grad_next, from_three.astype(jnp.float32))
    key_sum = own_sum[:, :kv_width]
    value_sum = own_sum[:, kv_width:]

    rows = jnp.concatenate(
        [
            query_acc.reshape(length, -1).astype(jnp.bfloat16),
            key_sum.astype(jnp.bfloat16),
            value_sum.astype(jnp.bfloat16),
        ],
        axis=1,
    )
    width = rows.shape[1]

    capacity = 2 * length // blocks
    own_targets = lax.dynamic_slice_in_dim(linear_row_index, block_index * length, length)
    target = own_targets // length
    owner_marks = (target[:, None] == lax.iota(jnp.int32, blocks)[None, :]).astype(jnp.int32)
    slot_rank = jnp.sum(owner_marks * (jnp.cumsum(owner_marks, axis=0) - 1), axis=1)
    send_slots = target * capacity + slot_rank
    pack = (
        lax.iota(jnp.int32, blocks * capacity)[:, None] == send_slots[None, :]
    ).astype(jnp.bfloat16)
    packed = jnp.dot(pack, rows, preferred_element_type=jnp.float32).astype(jnp.bfloat16)

    arrived = lax.all_to_all(packed, "ctx", split_axis=0, concat_axis=0, tiled=True)

    all_owners = linear_row_index.reshape(blocks, length)
    landing = all_owners // length == block_index
    landed_rank = jnp.cumsum(landing.astype(jnp.int32), axis=1) - 1
    where_to = all_owners % length
    chosen = landing[:, :, None] & (
        landed_rank[:, :, None] == lax.iota(jnp.int32, capacity)[None, None, :]
    )
    slot_pos = jnp.sum(jnp.where(chosen, where_to[:, :, None], 0), axis=1).reshape(-1)
    slot_valid = jnp.any(chosen, axis=1).reshape(-1)
    unpack = (
        (lax.iota(jnp.int32, length)[:, None] == slot_pos[None, :]) & slot_valid[None, :]
    ).astype(jnp.bfloat16)
    linear_rows = jnp.dot(unpack, arrived, preferred_element_type=jnp.float32).astype(
        jnp.bfloat16
    )

    gathered = lax.all_to_all(linear_rows, "head", split_axis=0, concat_axis=1, tiled=True)
    sub = length // heads_axis
    gathered = gathered.reshape(sub, heads_axis, width)
    query_out = gathered[:, :, :q_width].reshape(sub, heads_axis * q_width)
    key_out = gathered[:, :, q_width : q_width + kv_width].reshape(sub, heads_axis * kv_width)
    value_out = gathered[:, :, q_width + kv_width :].reshape(sub, heads_axis * kv_width)
    return query_out, key_out, value_out


def solution(mesh):
    placed = (
        P("ctx", "head"),
        P("ctx", "head"),
        P("ctx", "head"),
        P("ctx", "head"),
        P("ctx", "head"),
        P("head", "ctx"),
        P(),
        P(),
    )
    return jax.shard_map(
        per_device,
        mesh=mesh,
        in_specs=placed,
        out_specs=(P(("ctx", "head"), None), P(("ctx", "head"), None), P(("ctx", "head"), None)),
        check_vma=False,
    )
```

```python
import jax
import jax.numpy as jnp
from jax import lax
from jax.sharding import PartitionSpec as P


HEAD_SIZE = 128


def from_behind(shard, axis, by):
    count = lax.axis_size(axis)
    pairs = [(i, i + by) for i in range(count) if 0 <= i + by < count]
    return lax.ppermute(shard, axis, pairs)


def block_grads(
    query_vectors,
    output_gradient,
    log_normalizer,
    row_correction,
    begins,
    query_pos,
    key_heads,
    value_heads,
    key_start,
):
    length = query_vectors.shape[0]
    scaling = HEAD_SIZE ** (-0.5)
    scores = (
        jnp.einsum("qngd,knd->qngk", query_vectors, key_heads, preferred_element_type=jnp.float32)
        * scaling
    )
    key_pos = key_start + lax.iota(jnp.int32, length)
    visible = (key_pos[None, :] <= query_pos[:, None]) & (key_pos[None, :] >= begins[:, None])
    weights = jnp.exp(
        jnp.where(visible[:, None, None, :], scores - log_normalizer[..., None], -jnp.inf)
    )
    weights_low = weights.astype(jnp.bfloat16)
    grad_weights = jnp.einsum(
        "qngd,knd->qngk", output_gradient, value_heads, preferred_element_type=jnp.float32
    )
    grad_scores = (weights * (grad_weights - row_correction[..., None]) * scaling).astype(
        jnp.bfloat16
    )
    query_term = jnp.einsum(
        "qngk,knd->qngd", grad_scores, key_heads, preferred_element_type=jnp.float32
    )
    key_term = jnp.einsum(
        "qngk,qngd->knd", grad_scores, query_vectors, preferred_element_type=jnp.float32
    )
    value_term = jnp.einsum(
        "qngk,qngd->knd", weights_low, output_gradient, preferred_element_type=jnp.float32
    )
    return query_term, key_term.reshape(length, -1), value_term.reshape(length, -1)


def per_device(
    query_head_rows,
    key_head_rows,
    value_head_rows,
    forward_output,
    cotangent,
    logsumexp,
    document_lengths,
    linear_row_index,
):
    length = query_head_rows.shape[0]
    kv_heads = key_head_rows.shape[1] // HEAD_SIZE
    kv_width = key_head_rows.shape[1]
    q_width = query_head_rows.shape[1]
    query_groups = logsumexp.shape[0] // kv_heads
    block_index = lax.axis_index("ctx")
    blocks = lax.axis_size("ctx")
    heads_axis = lax.axis_size("head")

    kv_own = jnp.concatenate([key_head_rows, value_head_rows], axis=1)
    even = block_index % 2 == 0
    partner = [(i, i ^ 1) for i in range(blocks)]
    kv_two = from_behind(kv_own, "ctx", 2)
    kv_three = lax.ppermute(
        kv_own, "ctx", [(i, i + 3) for i in range(1, blocks, 2) if i + 3 < blocks]
    )

    def query_side(index, rows_q, rows_do, lse, correction):
        positions = index * length + lax.iota(jnp.int32, length)
        finish = jnp.cumsum(document_lengths)
        firsts = finish - document_lengths
        starts = jnp.max(
            jnp.where(firsts[None, :] <= positions[:, None], firsts[None, :], 0), axis=1
        )
        return (
            rows_q.reshape(length, kv_heads, query_groups, HEAD_SIZE),
            rows_do.reshape(length, kv_heads, query_groups, HEAD_SIZE),
            lse.T.reshape(length, kv_heads, query_groups),
            correction,
            starts,
            positions,
        )

    row_correction = jnp.sum(
        cotangent.reshape(length, kv_heads, query_groups, HEAD_SIZE).astype(jnp.float32)
        * forward_output.reshape(length, kv_heads, query_groups, HEAD_SIZE).astype(jnp.float32),
        axis=3,
    )
    mine = query_side(block_index, query_head_rows, cotangent, logsumexp, row_correction)
    their_q = lax.ppermute(query_head_rows, "ctx", partner)
    their_do = lax.ppermute(cotangent, "ctx", partner)
    their_high = lax.ppermute(
        jnp.concatenate([logsumexp, row_correction.reshape(length, -1).T], axis=0),
        "ctx",
        partner,
    )
    theirs = query_side(
        block_index ^ 1,
        their_q,
        their_do,
        their_high[: logsumexp.shape[0]],
        their_high[logsumexp.shape[0] :].T.reshape(row_correction.shape),
    )

    def block_terms(side, kv_part, key_block):
        key_heads = kv_part[:, :kv_width].reshape(length, kv_heads, HEAD_SIZE)
        value_heads = kv_part[:, kv_width:].reshape(length, kv_heads, HEAD_SIZE)
        query_term, key_term, value_term = block_grads(
            *side, key_heads, value_heads, key_block * length
        )
        return query_term, jnp.concatenate([key_term, value_term], axis=1)

    q_own, kv_grad_own = block_terms(mine, kv_own, block_index)
    q_two, kv_grad_two = block_terms(mine, kv_two, block_index - 2)
    q_cross, kv_grad_cross = block_terms(theirs, kv_two, block_index - 2)
    q_three, kv_grad_three = block_terms(mine, kv_three, block_index - 3)
    q_next, kv_grad_next = block_terms(theirs, kv_own, block_index)

    zero_q = jnp.zeros_like(q_own)
    zero_kv = jnp.zeros_like(kv_grad_own)
    sent_q = q_cross + jnp.where(even, q_next, zero_q)
    back_q = lax.ppermute(sent_q, "ctx", partner)
    query_acc = q_own + q_two + jnp.where(even, q_three, zero_q) + back_q

    crossed = from_behind((kv_grad_two + kv_grad_cross).astype(jnp.bfloat16), "ctx", -2)
    from_three = lax.ppermute(
        kv_grad_three.astype(jnp.bfloat16),
        "ctx",
        [(i, i - 3) for i in range(0, blocks, 2) if i >= 3],
    )
    own_sum = kv_grad_own + crossed.astype(jnp.float32)
    own_sum = own_sum + jnp.where(even, kv_grad_next, from_three.astype(jnp.float32))
    key_sum = own_sum[:, :kv_width]
    value_sum = own_sum[:, kv_width:]

    rows = jnp.concatenate(
        [
            query_acc.reshape(length, -1).astype(jnp.bfloat16),
            key_sum.astype(jnp.bfloat16),
            value_sum.astype(jnp.bfloat16),
        ],
        axis=1,
    )
    width = rows.shape[1]

    capacity = 2 * length // blocks
    own_targets = lax.dynamic_slice_in_dim(linear_row_index, block_index * length, length)
    target = own_targets // length
    owner_marks = (target[:, None] == lax.iota(jnp.int32, blocks)[None, :]).astype(jnp.int32)
    slot_rank = jnp.sum(owner_marks * (jnp.cumsum(owner_marks, axis=0) - 1), axis=1)
    send_slots = target * capacity + slot_rank
    pack = (
        lax.iota(jnp.int32, blocks * capacity)[:, None] == send_slots[None, :]
    ).astype(jnp.bfloat16)
    packed = jnp.dot(pack, rows, preferred_element_type=jnp.float32).astype(jnp.bfloat16)

    arrived = lax.all_to_all(packed, "ctx", split_axis=0, concat_axis=0, tiled=True)

    all_owners = linear_row_index.reshape(blocks, length)
    landing = all_owners // length == block_index
    landed_rank = jnp.cumsum(landing.astype(jnp.int32), axis=1) - 1
    where_to = all_owners % length
    chosen = landing[:, :, None] & (
        landed_rank[:, :, None] == lax.iota(jnp.int32, capacity)[None, None, :]
    )
    slot_pos = jnp.sum(jnp.where(chosen, where_to[:, :, None], 0), axis=1).reshape(-1)
    slot_valid = jnp.any(chosen, axis=1).reshape(-1)
    unpack = (
        (lax.iota(jnp.int32, length)[:, None] == slot_pos[None, :]) & slot_valid[None, :]
    ).astype(jnp.bfloat16)
    linear_rows = jnp.dot(unpack, arrived, preferred_element_type=jnp.float32).astype(
        jnp.bfloat16
    )

    gathered = lax.all_to_all(linear_rows, "head", split_axis=0, concat_axis=1, tiled=True)
    sub = length // heads_axis
    gathered = gathered.reshape(sub, heads_axis, width)
    query_out = gathered[:, :, :q_width].reshape(sub, heads_axis * q_width)
    key_out = gathered[:, :, q_width : q_width + kv_width].reshape(sub, heads_axis * kv_width)
    value_out = gathered[:, :, q_width + kv_width :].reshape(sub, heads_axis * kv_width)
    return query_out, key_out, value_out


def solution(mesh):
    placed = (
        P("ctx", "head"),
        P("ctx", "head"),
        P("ctx", "head"),
        P("ctx", "head"),
        P("ctx", "head"),
        P("head", "ctx"),
        P(),
        P(),
    )
    return jax.shard_map(
        per_device,
        mesh=mesh,
        in_specs=placed,
        out_specs=(P(("ctx", "head"), None), P(("ctx", "head"), None), P(("ctx", "head"), None)),
        check_vma=False,
    )
```

```python
import jax
import jax.numpy as jnp
from jax import lax
from jax.sharding import PartitionSpec as P


HEAD_SIZE = 128


def from_behind(shard, axis, by):
    count = lax.axis_size(axis)
    pairs = [(i, i + by) for i in range(count) if 0 <= i + by < count]
    return lax.ppermute(shard, axis, pairs)


def block_grads(
    query_vectors,
    output_gradient,
    log_normalizer,
    row_correction,
    begins,
    query_pos,
    key_heads,
    value_heads,
    key_start,
):
    length = query_vectors.shape[0]
    scaling = HEAD_SIZE ** (-0.5)
    scores = (
        jnp.einsum("qngd,knd->qngk", query_vectors, key_heads, preferred_element_type=jnp.float32)
        * scaling
    )
    key_pos = key_start + lax.iota(jnp.int32, length)
    visible = (key_pos[None, :] <= query_pos[:, None]) & (key_pos[None, :] >= begins[:, None])
    weights = jnp.exp(
        jnp.where(visible[:, None, None, :], scores - log_normalizer[..., None], -jnp.inf)
    )
    weights_low = weights.astype(jnp.bfloat16)
    grad_weights = jnp.einsum(
        "qngd,knd->qngk", output_gradient, value_heads, preferred_element_type=jnp.float32
    )
    grad_scores = (weights * (grad_weights - row_correction[..., None]) * scaling).astype(
        jnp.bfloat16
    )
    query_term = jnp.einsum(
        "qngk,knd->qngd", grad_scores, key_heads, preferred_element_type=jnp.float32
    )
    key_term = jnp.einsum(
        "qngk,qngd->knd", grad_scores, query_vectors, preferred_element_type=jnp.float32
    )
    value_term = jnp.einsum(
        "qngk,qngd->knd", weights_low, output_gradient, preferred_element_type=jnp.float32
    )
    return query_term, key_term.reshape(length, -1), value_term.reshape(length, -1)


def per_device(
    query_head_rows,
    key_head_rows,
    value_head_rows,
    forward_output,
    cotangent,
    logsumexp,
    document_lengths,
    linear_row_index,
):
    length = query_head_rows.shape[0]
    kv_heads = key_head_rows.shape[1] // HEAD_SIZE
    kv_width = key_head_rows.shape[1]
    q_width = query_head_rows.shape[1]
    query_groups = logsumexp.shape[0] // kv_heads
    block_index = lax.axis_index("ctx")
    blocks = lax.axis_size("ctx")
    heads_axis = lax.axis_size("head")

    kv_own = jnp.concatenate([key_head_rows, value_head_rows], axis=1)
    even = block_index % 2 == 0
    partner = [(i, i ^ 1) for i in range(blocks)]
    kv_two = from_behind(kv_own, "ctx", 2)
    kv_three = lax.ppermute(
        kv_own, "ctx", [(i, i + 3) for i in range(1, blocks, 2) if i + 3 < blocks]
    )

    def query_side(index, rows_q, rows_do, lse, correction):
        positions = index * length + lax.iota(jnp.int32, length)
        finish = jnp.cumsum(document_lengths)
        firsts = finish - document_lengths
        starts = jnp.max(
            jnp.where(firsts[None, :] <= positions[:, None], firsts[None, :], 0), axis=1
        )
        return (
            rows_q.reshape(length, kv_heads, query_groups, HEAD_SIZE),
            rows_do.reshape(length, kv_heads, query_groups, HEAD_SIZE),
            lse.T.reshape(length, kv_heads, query_groups),
            correction,
            starts,
            positions,
        )

    row_correction = jnp.sum(
        cotangent.reshape(length, kv_heads, query_groups, HEAD_SIZE).astype(jnp.float32)
        * forward_output.reshape(length, kv_heads, query_groups, HEAD_SIZE).astype(jnp.float32),
        axis=3,
    )
    mine = query_side(block_index, query_head_rows, cotangent, logsumexp, row_correction)
    their_low = lax.ppermute(jnp.concatenate([query_head_rows, cotangent], axis=1), "ctx", partner)
    their_high = lax.ppermute(
        jnp.concatenate([logsumexp, row_correction.reshape(length, -1).T], axis=0),
        "ctx",
        partner,
    )
    theirs = query_side(
        block_index ^ 1,
        their_low[:, :q_width],
        their_low[:, q_width:],
        their_high[: logsumexp.shape[0]],
        their_high[logsumexp.shape[0] :].T.reshape(row_correction.shape),
    )

    def block_terms(side, kv_part, key_block):
        key_heads = kv_part[:, :kv_width].reshape(length, kv_heads, HEAD_SIZE)
        value_heads = kv_part[:, kv_width:].reshape(length, kv_heads, HEAD_SIZE)
        query_term, key_term, value_term = block_grads(
            *side, key_heads, value_heads, key_block * length
        )
        return query_term, jnp.concatenate([key_term, value_term], axis=1)

    q_own, kv_grad_own = block_terms(mine, kv_own, block_index)
    q_two, kv_grad_two = block_terms(mine, kv_two, block_index - 2)
    q_cross, kv_grad_cross = block_terms(theirs, kv_two, block_index - 2)
    q_three, kv_grad_three = block_terms(mine, kv_three, block_index - 3)
    q_next, kv_grad_next = block_terms(theirs, kv_own, block_index)

    zero_q = jnp.zeros_like(q_own)
    zero_kv = jnp.zeros_like(kv_grad_own)
    sent_q = q_cross + jnp.where(even, q_next, zero_q)
    back_q = lax.ppermute(sent_q, "ctx", partner)
    query_acc = q_own + q_two + jnp.where(even, q_three, zero_q) + back_q

    crossed = from_behind((kv_grad_two + kv_grad_cross).astype(jnp.bfloat16), "ctx", -2)
    from_three = lax.ppermute(
        kv_grad_three.astype(jnp.bfloat16),
        "ctx",
        [(i, i - 3) for i in range(0, blocks, 2) if i >= 3],
    )
    own_sum = kv_grad_own + crossed.astype(jnp.float32)
    own_sum = own_sum + jnp.where(even, kv_grad_next, from_three.astype(jnp.float32))
    key_sum = own_sum[:, :kv_width]
    value_sum = own_sum[:, kv_width:]

    rows = jnp.concatenate(
        [
            query_acc.reshape(length, -1).astype(jnp.bfloat16),
            key_sum.astype(jnp.bfloat16),
            value_sum.astype(jnp.bfloat16),
        ],
        axis=1,
    )
    width = rows.shape[1]

    capacity = 2 * length // blocks
    own_targets = lax.dynamic_slice_in_dim(linear_row_index, block_index * length, length)
    target = own_targets // length
    owner_marks = (target[:, None] == lax.iota(jnp.int32, blocks)[None, :]).astype(jnp.int32)
    slot_rank = jnp.sum(owner_marks * (jnp.cumsum(owner_marks, axis=0) - 1), axis=1)
    send_slots = target * capacity + slot_rank
    pack = (
        lax.iota(jnp.int32, blocks * capacity)[:, None] == send_slots[None, :]
    ).astype(jnp.bfloat16)
    packed_q = jnp.dot(pack, rows[:, :q_width], preferred_element_type=jnp.float32)
    arrived_q = lax.all_to_all(
        packed_q.astype(jnp.bfloat16), "ctx", split_axis=0, concat_axis=0, tiled=True
    )
    packed_kv = jnp.dot(pack, rows[:, q_width:], preferred_element_type=jnp.float32)
    arrived_kv = lax.all_to_all(
        packed_kv.astype(jnp.bfloat16), "ctx", split_axis=0, concat_axis=0, tiled=True
    )
    arrived = jnp.concatenate([arrived_q, arrived_kv], axis=1)

    all_owners = linear_row_index.reshape(blocks, length)
    landing = all_owners // length == block_index
    landed_rank = jnp.cumsum(landing.astype(jnp.int32), axis=1) - 1
    where_to = all_owners % length
    chosen = landing[:, :, None] & (
        landed_rank[:, :, None] == lax.iota(jnp.int32, capacity)[None, None, :]
    )
    slot_pos = jnp.sum(jnp.where(chosen, where_to[:, :, None], 0), axis=1).reshape(-1)
    slot_valid = jnp.any(chosen, axis=1).reshape(-1)
    unpack = (
        (lax.iota(jnp.int32, length)[:, None] == slot_pos[None, :]) & slot_valid[None, :]
    ).astype(jnp.bfloat16)
    linear_rows = jnp.dot(unpack, arrived, preferred_element_type=jnp.float32).astype(
        jnp.bfloat16
    )

    gathered = lax.all_to_all(linear_rows, "head", split_axis=0, concat_axis=1, tiled=True)
    sub = length // heads_axis
    gathered = gathered.reshape(sub, heads_axis, width)
    query_out = gathered[:, :, :q_width].reshape(sub, heads_axis * q_width)
    key_out = gathered[:, :, q_width : q_width + kv_width].reshape(sub, heads_axis * kv_width)
    value_out = gathered[:, :, q_width + kv_width :].reshape(sub, heads_axis * kv_width)
    return query_out, key_out, value_out


def solution(mesh):
    placed = (
        P("ctx", "head"),
        P("ctx", "head"),
        P("ctx", "head"),
        P("ctx", "head"),
        P("ctx", "head"),
        P("head", "ctx"),
        P(),
        P(),
    )
    return jax.shard_map(
        per_device,
        mesh=mesh,
        in_specs=placed,
        out_specs=(P(("ctx", "head"), None), P(("ctx", "head"), None), P(("ctx", "head"), None)),
        check_vma=False,
    )
```

```python
import jax
import jax.numpy as jnp
from jax import lax
from jax.sharding import PartitionSpec as P


HEAD_SIZE = 128


def from_behind(shard, axis, by):
    count = lax.axis_size(axis)
    pairs = [(i, i + by) for i in range(count) if 0 <= i + by < count]
    return lax.ppermute(shard, axis, pairs)


def block_grads(
    query_vectors,
    output_gradient,
    log_normalizer,
    row_correction,
    begins,
    query_pos,
    key_heads,
    value_heads,
    key_start,
):
    length = query_vectors.shape[0]
    scaling = HEAD_SIZE ** (-0.5)
    scores = (
        jnp.einsum("qngd,knd->qngk", query_vectors, key_heads, preferred_element_type=jnp.float32)
        * scaling
    )
    key_pos = key_start + lax.iota(jnp.int32, length)
    visible = (key_pos[None, :] <= query_pos[:, None]) & (key_pos[None, :] >= begins[:, None])
    weights = jnp.exp(
        jnp.where(visible[:, None, None, :], scores - log_normalizer[..., None], -jnp.inf)
    )
    weights_low = weights.astype(jnp.bfloat16)
    grad_weights = jnp.einsum(
        "qngd,knd->qngk", output_gradient, value_heads, preferred_element_type=jnp.float32
    )
    grad_scores = (weights * (grad_weights - row_correction[..., None]) * scaling).astype(
        jnp.bfloat16
    )
    query_term = jnp.einsum(
        "qngk,knd->qngd", grad_scores, key_heads, preferred_element_type=jnp.float32
    )
    key_term = jnp.einsum(
        "qngk,qngd->knd", grad_scores, query_vectors, preferred_element_type=jnp.float32
    )
    value_term = jnp.einsum(
        "qngk,qngd->knd", weights_low, output_gradient, preferred_element_type=jnp.float32
    )
    return query_term, key_term.reshape(length, -1), value_term.reshape(length, -1)


def per_device(
    query_head_rows,
    key_head_rows,
    value_head_rows,
    forward_output,
    cotangent,
    logsumexp,
    document_lengths,
    linear_row_index,
):
    length = query_head_rows.shape[0]
    kv_heads = key_head_rows.shape[1] // HEAD_SIZE
    kv_width = key_head_rows.shape[1]
    q_width = query_head_rows.shape[1]
    query_groups = logsumexp.shape[0] // kv_heads
    block_index = lax.axis_index("ctx")
    blocks = lax.axis_size("ctx")
    heads_axis = lax.axis_size("head")

    kv_own = jnp.concatenate([key_head_rows, value_head_rows], axis=1)
    even = block_index % 2 == 0
    partner = [(i, i ^ 1) for i in range(blocks)]
    kv_two = from_behind(kv_own, "ctx", 2)
    kv_three = lax.ppermute(
        kv_own, "ctx", [(i, i + 3) for i in range(1, blocks, 2) if i + 3 < blocks]
    )

    def query_side(index, rows_q, rows_do, lse, correction):
        positions = index * length + lax.iota(jnp.int32, length)
        finish = jnp.cumsum(document_lengths)
        firsts = finish - document_lengths
        starts = jnp.max(
            jnp.where(firsts[None, :] <= positions[:, None], firsts[None, :], 0), axis=1
        )
        return (
            rows_q.reshape(length, kv_heads, query_groups, HEAD_SIZE),
            rows_do.reshape(length, kv_heads, query_groups, HEAD_SIZE),
            lse.T.reshape(length, kv_heads, query_groups),
            correction,
            starts,
            positions,
        )

    row_correction = jnp.sum(
        cotangent.reshape(length, kv_heads, query_groups, HEAD_SIZE).astype(jnp.float32)
        * forward_output.reshape(length, kv_heads, query_groups, HEAD_SIZE).astype(jnp.float32),
        axis=3,
    )
    mine = query_side(block_index, query_head_rows, cotangent, logsumexp, row_correction)
    their_low = lax.ppermute(jnp.concatenate([query_head_rows, cotangent], axis=1), "ctx", partner)
    their_high = lax.ppermute(
        jnp.concatenate([logsumexp, row_correction.reshape(length, -1).T], axis=0),
        "ctx",
        partner,
    )
    theirs = query_side(
        block_index ^ 1,
        their_low[:, :q_width],
        their_low[:, q_width:],
        their_high[: logsumexp.shape[0]],
        their_high[logsumexp.shape[0] :].T.reshape(row_correction.shape),
    )

    def block_terms(side, kv_part, key_block):
        key_heads = kv_part[:, :kv_width].reshape(length, kv_heads, HEAD_SIZE)
        value_heads = kv_part[:, kv_width:].reshape(length, kv_heads, HEAD_SIZE)
        query_term, key_term, value_term = block_grads(
            *side, key_heads, value_heads, key_block * length
        )
        return query_term, jnp.concatenate([key_term, value_term], axis=1)

    q_own, kv_grad_own = block_terms(mine, kv_own, block_index)
    q_two, kv_grad_two = block_terms(mine, kv_two, block_index - 2)
    q_cross, kv_grad_cross = block_terms(theirs, kv_two, block_index - 2)
    q_three, kv_grad_three = block_terms(mine, kv_three, block_index - 3)
    q_next, kv_grad_next = block_terms(theirs, kv_own, block_index)

    zero_q = jnp.zeros_like(q_own)
    zero_kv = jnp.zeros_like(kv_grad_own)
    sent_q = q_cross + jnp.where(even, q_next, zero_q)
    back_q = lax.ppermute(sent_q.astype(jnp.bfloat16), "ctx", partner).astype(jnp.float32)
    query_acc = q_own + q_two + jnp.where(even, q_three, zero_q) + back_q

    crossed = from_behind((kv_grad_two + kv_grad_cross).astype(jnp.bfloat16), "ctx", -2)
    from_three = lax.ppermute(
        kv_grad_three.astype(jnp.bfloat16),
        "ctx",
        [(i, i - 3) for i in range(0, blocks, 2) if i >= 3],
    )
    own_sum = kv_grad_own + crossed.astype(jnp.float32)
    own_sum = own_sum + jnp.where(even, kv_grad_next, from_three.astype(jnp.float32))
    key_sum = own_sum[:, :kv_width]
    value_sum = own_sum[:, kv_width:]

    rows = jnp.concatenate(
        [
            query_acc.reshape(length, -1).astype(jnp.bfloat16),
            key_sum.astype(jnp.bfloat16),
            value_sum.astype(jnp.bfloat16),
        ],
        axis=1,
    )
    width = rows.shape[1]

    capacity = 2 * length // blocks
    own_targets = lax.dynamic_slice_in_dim(linear_row_index, block_index * length, length)
    target = own_targets // length
    owner_marks = (target[:, None] == lax.iota(jnp.int32, blocks)[None, :]).astype(jnp.int32)
    slot_rank = jnp.sum(owner_marks * (jnp.cumsum(owner_marks, axis=0) - 1), axis=1)
    send_slots = target * capacity + slot_rank
    pack = (
        lax.iota(jnp.int32, blocks * capacity)[:, None] == send_slots[None, :]
    ).astype(jnp.bfloat16)
    packed = jnp.dot(pack, rows, preferred_element_type=jnp.float32).astype(jnp.bfloat16)

    arrived = lax.all_to_all(packed, "ctx", split_axis=0, concat_axis=0, tiled=True)

    all_owners = linear_row_index.reshape(blocks, length)
    landing = all_owners // length == block_index
    landed_rank = jnp.cumsum(landing.astype(jnp.int32), axis=1) - 1
    where_to = all_owners % length
    chosen = landing[:, :, None] & (
        landed_rank[:, :, None] == lax.iota(jnp.int32, capacity)[None, None, :]
    )
    slot_pos = jnp.sum(jnp.where(chosen, where_to[:, :, None], 0), axis=1).reshape(-1)
    slot_valid = jnp.any(chosen, axis=1).reshape(-1)
    unpack = (
        (lax.iota(jnp.int32, length)[:, None] == slot_pos[None, :]) & slot_valid[None, :]
    ).astype(jnp.bfloat16)
    linear_rows = jnp.dot(unpack, arrived, preferred_element_type=jnp.float32).astype(
        jnp.bfloat16
    )

    gathered = lax.all_to_all(linear_rows, "head", split_axis=0, concat_axis=1, tiled=True)
    sub = length // heads_axis
    gathered = gathered.reshape(sub, heads_axis, width)
    query_out = gathered[:, :, :q_width].reshape(sub, heads_axis * q_width)
    key_out = gathered[:, :, q_width : q_width + kv_width].reshape(sub, heads_axis * kv_width)
    value_out = gathered[:, :, q_width + kv_width :].reshape(sub, heads_axis * kv_width)
    return query_out, key_out, value_out


def solution(mesh):
    placed = (
        P("ctx", "head"),
        P("ctx", "head"),
        P("ctx", "head"),
        P("ctx", "head"),
        P("ctx", "head"),
        P("head", "ctx"),
        P(),
        P(),
    )
    return jax.shard_map(
        per_device,
        mesh=mesh,
        in_specs=placed,
        out_specs=(P(("ctx", "head"), None), P(("ctx", "head"), None), P(("ctx", "head"), None)),
        check_vma=False,
    )
```
